512 devices in a mesh: seg: 32 (over z, core), row: 16 (over x, y).
Axes of the slice: x: 4, y: 4, z: 16, core: 2. Of those that a mesh axis runs over, the one named last changes fastest.
Arguments:
- basis: bfloat16 [32, 8192, 1024], P('seg', 'row'), may hold values from -6 to 6
- arriving: bfloat16 [8192, 1024], P('row'), may hold values from -6 to 6
- blocks: bfloat16 [32, 8192, 256], P('seg', 'row'), may hold values from -8 to 8
- pattern: int32 [32, 128, 4], P('seg', 'row'), may hold values from 0 to 127, as said below
- growth: float32 [32, 1024], P('seg'), may hold values from -6 to 6
Outputs:
- next_basis: bfloat16 [32, 8192, 1024], P('seg', 'row')
- next_growth: float32 [32, 1024], P('seg')
The draws below stay inside these ranges and needn't reach their ends.
Inputs may be any that keep to these rules, and one draw needn't show every extreme that they name: `pattern`: entry 0 of block row r is r itself; entry 1 is the block 4 positions before or after r on the cycle of 128 blocks; the other entries are distinct blocks fewer than 4 positions from r and not r.
All inputs are finite; a program needn't handle non-finite values.
Results may differ from the reference program's by a relative error of at most 0.0053.
Values may be sent and summed in bfloat16 or wider, within the bound.
No kernel may reach another device: no remote copies, remote signals or barrier semaphores. Data moves between devices by JAX's collectives and lax.ppermute only.
A program may use at most 128 MiB of HBM per device.

```python
import math
import jax
import jax.numpy as jnp
from jax import lax

NCH = 8192
K = 1024
BS = 64
NB = 4
REACH = 4
SEGS = 32
NBLK = 128


def draw_blocks(key, part):
    key_gain, key_raw = jax.random.split(key, 2)
    gains = jnp.exp(jax.random.uniform(key_gain, (SEGS, NCH, 1), minval=math.log(0.5), maxval=math.log(2.0)))
    raw_values = jax.random.uniform(key_raw, (SEGS, NCH, NB * BS), minval=-1.0, maxval=1.0)
    coupling = raw_values * (3.0 / (NB * BS))
    column_ids = jnp.arange(NB * BS)
    row_places = jnp.arange(NCH) % BS
    on_diagonal = column_ids[None, :] == row_places[:, None]
    entries = jnp.where(on_diagonal[None], 4.0, coupling) * gains
    return entries.astype(jnp.float32).astype(jnp.bfloat16)


def draw_pattern(key, part):
    key_sign, key_score = jax.random.split(key, 2)
    far_sign = jax.random.randint(key_sign, (SEGS, NBLK, 1), 0, 2) * 2 - 1
    far_offset = far_sign * REACH
    candidates = jnp.concatenate([jnp.arange(1 - REACH, 0), jnp.arange(1, REACH)]).astype(jnp.int32)
    scores = jax.random.randint(key_score, (SEGS, NBLK, 2 * REACH - 2), 0, 65536) * (2 * REACH - 2) + jnp.arange(2 * REACH - 2)
    ordering = jnp.argsort(scores, axis=-1, stable=True)
    chosen = candidates[ordering[..., :NB - 2]]
    offsets = jnp.concatenate([jnp.zeros((SEGS, NBLK, 1), jnp.int32), far_offset.astype(jnp.int32), chosen.astype(jnp.int32)], axis=-1)
    own_blocks = jnp.arange(NBLK, dtype=jnp.int32)[None, :, None]
    return ((own_blocks + offsets) % NBLK).astype(jnp.int32)


def block_scale(stream_key, dims, shards, low, top_value):
    factor_of = 1.0
    for position, shards_of in shards:
        heights = jax.random.uniform(jax.random.fold_in(jax.random.fold_in(stream_key, 6), position), (shards_of,), jnp.float32, low / len(shards), top_value / len(shards))
        factor_of = factor_of * jnp.repeat(jnp.exp(heights), dims[position] // shards_of).reshape((-1,) + (1,) * (len(dims) - 1 - position))
    return factor_of


def scatter_about(rng, extent, width, bound, pieces=(), held_as=jnp.bfloat16):
    loudness = block_scale(rng, extent, pieces, -0.22, 0.18) if pieces else 1.0
    result = jax.random.normal(rng, extent, jnp.float32) * width * loudness
    return jnp.minimum(jnp.maximum(result, -bound), bound).astype(held_as)


def setup_inputs(seed: int = 0) -> dict:
    arg_keys = jax.random.split(jax.random.key(seed), 6)
    basis = scatter_about(arg_keys[0], (SEGS, NCH, K), 1.0, 6.0, ((0, 32), (1, 16)))
    arriving = scatter_about(arg_keys[1], (NCH, K), 1.0, 6.0, ((0, 16),))
    blocks = draw_blocks(jax.random.fold_in(arg_keys[5], 71), 0)
    pattern = draw_pattern(jax.random.fold_in(arg_keys[5], 71), 0)
    growth = scatter_about(arg_keys[4], (SEGS, K), 1.0, 6.0, ((0, 32),), jnp.float32)
    return dict(basis=basis, arriving=arriving, blocks=blocks, pattern=pattern, growth=growth)


def advance(section_basis, section_blocks, section_pattern, section_growth):
    tile_stack = section_basis.reshape(NCH // BS, BS, K)
    picked = tile_stack[section_pattern]
    values = section_blocks.reshape(NCH // BS, BS, NB, BS)
    propagated = jnp.einsum('rinj,rnjk->rik', values.astype(jnp.float32), picked.astype(jnp.float32))
    propagated = propagated.reshape(NCH, K).astype(jnp.bfloat16)
    gram_matrix = jnp.dot(propagated.T.astype(jnp.float32), propagated.astype(jnp.float32), preferred_element_type=jnp.float32) / NCH
    factor = jnp.linalg.cholesky(gram_matrix)
    grown = section_growth + jnp.log(jnp.diagonal(factor))
    renewed = lax.linalg.triangular_solve(factor, propagated.astype(jnp.float32), left_side=False, lower=True, transpose_a=True)
    return (renewed.astype(jnp.bfloat16), grown)

def reference(basis, arriving, blocks, pattern, growth):
    renewed, grown = lax.map(lambda section_items: advance(*section_items), (basis, blocks, pattern, growth))
    next_basis = jnp.concatenate([arriving[None], renewed[:-1]], axis=0)
    return (next_basis, grown)
```

```python
import jax
import jax.numpy as jnp
from jax import lax
from jax.sharding import PartitionSpec as P

BS = 64
NB = 4
REACH = 4
PANEL = 128
HIGHEST = lax.Precision.HIGHEST


def padded_2(block, sides, width):
    for axis, dim in sides:
        count = lax.axis_size(axis)
        forward = [(i, i + 1) for i in range(count - 1)]
        forward.append((count - 1, 0))
        backward = [(target, source) for source, target in forward]
        low = lax.ppermute(
            lax.slice_in_dim(block, block.shape[dim] - width, None, axis=dim), axis, forward
        )
        high = lax.ppermute(lax.slice_in_dim(block, 0, width, axis=dim), axis, backward)
        block = jnp.concatenate([low, block, high], axis=dim)
    return block


def shifted(array, axis, by):
    length = lax.axis_size(axis)
    pairs = [(i, i + by) for i in range(length) if 0 <= i + by < length]
    return lax.ppermute(array, axis, pairs)


def times_t(a, b):
    return lax.dot_general(
        a, b, (((1,), (1,)), ((), ())), precision=HIGHEST, preferred_element_type=jnp.float32
    )


def body(basis, arriving, blocks, pattern, growth):
    row_count = basis.shape[1]
    col_count = basis.shape[2]
    row_blocks = row_count // BS
    total_blocks = row_blocks * lax.axis_size("row")
    padded = padded_2(basis[0], (("row", 0),), REACH * BS)
    tile_stack = padded.reshape(row_blocks + 2 * REACH, BS, col_count)
    local_ids = jnp.arange(row_blocks, dtype=jnp.int32)
    own_blocks = lax.axis_index("row") * row_blocks + local_ids
    offsets = (pattern[0] - own_blocks[:, None] + REACH) % total_blocks
    picked = jnp.take(tile_stack, local_ids[:, None] + offsets, axis=0)
    values = blocks[0].reshape(row_blocks, BS, NB, BS)
    propagated = jnp.einsum("rinj,rnjk->rik", values, picked, preferred_element_type=jnp.float32)
    propagated = propagated.reshape(row_count, col_count).astype(jnp.bfloat16)
    wide_rows = propagated.astype(jnp.float32)
    scale = 1.0 / (row_count * lax.axis_size("row"))

    width = PANEL
    panels = col_count // width
    eye = jnp.eye(width, dtype=jnp.float32)
    columns = []
    solved = []
    logs = []
    previous = None
    for k in range(panels):
        low = k * width
        part = lax.dot_general(
            propagated[:, low:],
            propagated[:, low:low + width],
            (((0,), (0,)), ((), ())),
            preferred_element_type=jnp.float32,
        )
        if previous is not None:
            part = part + previous[0, 0] * 0.0
        panel = lax.psum(part, "row") * scale
        previous = panel
        if k:
            left = jnp.concatenate(
                [column[low - j * width:] for j, column in enumerate(columns)], axis=1
            )
            panel = panel - times_t(left, left[:width])
        diag = jnp.linalg.cholesky(panel[:width])
        inverse = lax.linalg.triangular_solve(diag, eye, left_side=True, lower=True)
        logs.append(jnp.log(jnp.sum(diag * eye, axis=0)))
        if low + width < col_count:
            below = times_t(panel[width:], inverse)
            columns.append(jnp.concatenate([diag, below], axis=0))
        else:
            columns.append(diag)
        rhs = wide_rows[:, low:low + width]
        if k:
            rhs = rhs - times_t(jnp.concatenate(solved, axis=1), left[:width])
        solved.append(times_t(rhs, inverse))

    next_growth = growth + jnp.concatenate(logs)[None, :]
    renewed = jnp.concatenate(solved, axis=1)
    first_section = lax.axis_index("seg") == 0
    received = shifted(renewed.astype(jnp.bfloat16)[None], "seg", 1)
    next_basis = jnp.where(first_section, arriving[None], received)
    return (next_basis, next_growth)


def solution(mesh):
    return jax.shard_map(
        body,
        mesh=mesh,
        in_specs=(
            P("seg", "row", None),
            P("row", None),
            P("seg", "row", None),
            P("seg", "row", None),
            P("seg", None),
        ),
        out_specs=(P("seg", "row", None), P("seg", None)),
        check_vma=False,
    )
```

```python
import jax
import jax.numpy as jnp
from jax import lax
from jax.sharding import PartitionSpec as P

BS = 64
NB = 4
REACH = 4
PANEL = 128
HIGHEST = lax.Precision.HIGHEST


def padded_2(block, sides, width):
    for axis, dim in sides:
        count = lax.axis_size(axis)
        forward = [(i, i + 1) for i in range(count - 1)]
        forward.append((count - 1, 0))
        backward = [(target, source) for source, target in forward]
        low = lax.ppermute(
            lax.slice_in_dim(block, block.shape[dim] - width, None, axis=dim), axis, forward
        )
        high = lax.ppermute(lax.slice_in_dim(block, 0, width, axis=dim), axis, backward)
        block = jnp.concatenate([low, block, high], axis=dim)
    return block


def shifted(array, axis, by):
    length = lax.axis_size(axis)
    pairs = [(i, i + by) for i in range(length) if 0 <= i + by < length]
    return lax.ppermute(array, axis, pairs)


def times_t(a, b):
    return lax.dot_general(
        a, b, (((1,), (1,)), ((), ())), precision=HIGHEST, preferred_element_type=jnp.float32
    )


def body(basis, arriving, blocks, pattern, growth):
    row_count = basis.shape[1]
    col_count = basis.shape[2]
    row_blocks = row_count // BS
    total_blocks = row_blocks * lax.axis_size("row")
    padded = padded_2(basis[0], (("row", 0),), REACH * BS)
    tile_stack = padded.reshape(row_blocks + 2 * REACH, BS, col_count)
    local_ids = jnp.arange(row_blocks, dtype=jnp.int32)
    own_blocks = lax.axis_index("row") * row_blocks + local_ids
    offsets = (pattern[0] - own_blocks[:, None] + REACH) % total_blocks
    picked = jnp.take(tile_stack, local_ids[:, None] + offsets, axis=0)
    values = blocks[0].reshape(row_blocks, BS, NB, BS)
    propagated = jnp.einsum("rinj,rnjk->rik", values, picked, preferred_element_type=jnp.float32)
    propagated = propagated.reshape(row_count, col_count).astype(jnp.bfloat16)
    wide_rows = propagated.astype(jnp.float32)
    scale = 1.0 / (row_count * lax.axis_size("row"))

    partial_value = lax.dot_general(
        propagated, propagated, (((0,), (0,)), ((), ())), preferred_element_type=jnp.float32
    )
    gram_matrix = lax.psum(partial_value, "row") * scale

    width = PANEL
    panels = col_count // width
    eye = jnp.eye(width, dtype=jnp.float32)
    columns = []
    solved = []
    logs = []
    for k in range(panels):
        low = k * width
        panel = gram_matrix[low:, low:low + width]
        if k:
            left = jnp.concatenate(
                [column[low - j * width:] for j, column in enumerate(columns)], axis=1
            )
            panel = panel - times_t(left, left[:width])
        diag = jnp.linalg.cholesky(panel[:width])
        inverse = lax.linalg.triangular_solve(diag, eye, left_side=True, lower=True)
        logs.append(jnp.log(jnp.sum(diag * eye, axis=0)))
        if low + width < col_count:
            below = times_t(panel[width:], inverse)
            columns.append(jnp.concatenate([diag, below], axis=0))
        else:
            columns.append(diag)
        rhs = wide_rows[:, low:low + width]
        if k:
            rhs = rhs - times_t(jnp.concatenate(solved, axis=1), left[:width])
        solved.append(times_t(rhs, inverse))

    next_growth = growth + jnp.concatenate(logs)[None, :]
    renewed = jnp.concatenate(solved, axis=1)
    first_section = lax.axis_index("seg") == 0
    received = shifted(renewed.astype(jnp.bfloat16)[None], "seg", 1)
    next_basis = jnp.where(first_section, arriving[None], received)
    return (next_basis, next_growth)


def solution(mesh):
    return jax.shard_map(
        body,
        mesh=mesh,
        in_specs=(
            P("seg", "row", None),
            P("row", None),
            P("seg", "row", None),
            P("seg", "row", None),
            P("seg", None),
        ),
        out_specs=(P("seg", "row", None), P("seg", None)),
        check_vma=False,
    )
```

```python
import jax
import jax.numpy as jnp
from jax import lax
from jax.sharding import PartitionSpec as P
from jax.experimental import pallas as pl
from jax.experimental.pallas import tpu as pltpu


def _chol_inv_kernel(a_ref, lt_ref, x_ref):
    n = a_ref.shape[0]
    rows = 8
    nblk = n // rows
    a = [a_ref[b * rows:(b + 1) * rows, :] for b in range(nblk)]
    sub = lax.broadcasted_iota(jnp.int32, (rows, n), 0)
    lane1 = lax.broadcasted_iota(jnp.int32, (1, n), 1)
    x = [jnp.where(sub + b * rows == lax.broadcasted_iota(jnp.int32, (rows, n), 1), 1.0, 0.0).astype(jnp.float32)
         for b in range(nblk)]
    for j in range(n):
        bj, r = divmod(j, rows)
        row = a[bj][r:r + 1, :]
        d = row[:, j:j + 1]
        s = lax.rsqrt(d)
        lrow = jnp.where(lane1 >= j, row * s, 0.0)
        lt_ref[j:j + 1, :] = lrow
        xrow = x[bj][r:r + 1, :] * s
        for b in range(bj, nblk):
            col = a[b][:, j:j + 1] * s
            if b == bj:
                keep = sub >= r
                a[b] = jnp.where(keep, a[b] - col * lrow, a[b])
                x[b] = jnp.where(sub == r, xrow, jnp.where(sub > r, x[b] - col * xrow, x[b]))
            else:
                a[b] = a[b] - col * lrow
                x[b] = x[b] - col * xrow
    for b in range(nblk):
        x_ref[b * rows:(b + 1) * rows, :] = x[b]


def chol_inv(a):
    n = a.shape[0]
    return pl.pallas_call(
        _chol_inv_kernel,
        out_shape=(jax.ShapeDtypeStruct((n, n), jnp.float32), jax.ShapeDtypeStruct((n, n), jnp.float32)),
        in_specs=[pl.BlockSpec(memory_space=pltpu.VMEM)],
        out_specs=(pl.BlockSpec(memory_space=pltpu.VMEM), pl.BlockSpec(memory_space=pltpu.VMEM)),
    )(a)

BS = 64
NB = 4
REACH = 4
PANEL = 128
HIGHEST = lax.Precision.HIGHEST


def padded_2(block, sides, width):
    for axis, dim in sides:
        count = lax.axis_size(axis)
        forward = [(i, i + 1) for i in range(count - 1)]
        forward.append((count - 1, 0))
        backward = [(target, source) for source, target in forward]
        low = lax.ppermute(
            lax.slice_in_dim(block, block.shape[dim] - width, None, axis=dim), axis, forward
        )
        high = lax.ppermute(lax.slice_in_dim(block, 0, width, axis=dim), axis, backward)
        block = jnp.concatenate([low, block, high], axis=dim)
    return block


def shifted(array, axis, by):
    length = lax.axis_size(axis)
    pairs = [(i, i + by) for i in range(length) if 0 <= i + by < length]
    return lax.ppermute(array, axis, pairs)


def times_t(a, b):
    return lax.dot_general(
        a, b, (((1,), (1,)), ((), ())), precision=HIGHEST, preferred_element_type=jnp.float32
    )


def body(basis, arriving, blocks, pattern, growth):
    row_count = basis.shape[1]
    col_count = basis.shape[2]
    row_blocks = row_count // BS
    total_blocks = row_blocks * lax.axis_size("row")
    padded = padded_2(basis[0], (("row", 0),), REACH * BS)
    tile_stack = padded.reshape(row_blocks + 2 * REACH, BS, col_count)
    local_ids = jnp.arange(row_blocks, dtype=jnp.int32)
    own_blocks = lax.axis_index("row") * row_blocks + local_ids
    offsets = (pattern[0] - own_blocks[:, None] + REACH) % total_blocks
    picked = jnp.take(tile_stack, local_ids[:, None] + offsets, axis=0)
    values = blocks[0].reshape(row_blocks, BS, NB, BS)
    propagated = jnp.einsum("rinj,rnjk->rik", values, picked, preferred_element_type=jnp.float32)
    propagated = propagated.reshape(row_count, col_count).astype(jnp.bfloat16)
    wide_rows = propagated.astype(jnp.float32)
    scale = 1.0 / (row_count * lax.axis_size("row"))

    partial_value = lax.dot_general(
        propagated, propagated, (((0,), (0,)), ((), ())), preferred_element_type=jnp.float32
    )
    gram_matrix = lax.psum(partial_value, "row") * scale

    width = PANEL
    panels = col_count // width
    eye = jnp.eye(width, dtype=jnp.float32)
    columns = []
    solved = []
    logs = []
    for k in range(panels):
        low = k * width
        panel = gram_matrix[low:, low:low + width]
        if k:
            left = jnp.concatenate(
                [column[low - j * width:] for j, column in enumerate(columns)], axis=1
            )
            panel = panel - times_t(left, left[:width])
        block = panel[:width]
        upper, inverse = chol_inv((block + block.T) * 0.5)
        diag = upper.T
        logs.append(jnp.log(jnp.sum(diag * eye, axis=0)))
        if low + width < col_count:
            below = times_t(panel[width:], inverse)
            columns.append(jnp.concatenate([diag, below], axis=0))
        else:
            columns.append(diag)
        rhs = wide_rows[:, low:low + width]
        if k:
            rhs = rhs - times_t(jnp.concatenate(solved, axis=1), left[:width])
        solved.append(times_t(rhs, inverse))

    next_growth = growth + jnp.concatenate(logs)[None, :]
    renewed = jnp.concatenate(solved, axis=1)
    first_section = lax.axis_index("seg") == 0
    received = shifted(renewed.astype(jnp.bfloat16)[None], "seg", 1)
    next_basis = jnp.where(first_section, arriving[None], received)
    return (next_basis, next_growth)


def solution(mesh):
    return jax.shard_map(
        body,
        mesh=mesh,
        in_specs=(
            P("seg", "row", None),
            P("row", None),
            P("seg", "row", None),
            P("seg", "row", None),
            P("seg", None),
        ),
        out_specs=(P("seg", "row", None), P("seg", None)),
        check_vma=False,
    )
```

```python
import jax
import jax.numpy as jnp
from jax import lax
from jax.sharding import PartitionSpec as P
from jax.experimental import pallas as pl
from jax.experimental.pallas import tpu as pltpu


def _chol_inv_kernel(a_ref, lt_ref, x_ref):
    n = a_ref.shape[0]
    rows = 8
    nblk = n // rows
    a = [a_ref[b * rows:(b + 1) * rows, :] for b in range(nblk)]
    sub = lax.broadcasted_iota(jnp.int32, (rows, n), 0)
    lane1 = lax.broadcasted_iota(jnp.int32, (1, n), 1)
    x = [jnp.where(sub + b * rows == lax.broadcasted_iota(jnp.int32, (rows, n), 1), 1.0, 0.0).astype(jnp.float32)
         for b in range(nblk)]
    for j in range(n):
        bj, r = divmod(j, rows)
        row = a[bj][r:r + 1, :]
        d = row[:, j:j + 1]
        s = lax.rsqrt(d)
        lrow = jnp.where(lane1 >= j, row * s, 0.0)
        lt_ref[j:j + 1, :] = lrow
        xrow = x[bj][r:r + 1, :] * s
        for b in range(bj, nblk):
            col = a[b][:, j:j + 1] * s
            if b == bj:
                keep = sub >= r
                a[b] = jnp.where(keep, a[b] - col * lrow, a[b])
                x[b] = jnp.where(sub == r, xrow, jnp.where(sub > r, x[b] - col * xrow, x[b]))
            else:
                a[b] = a[b] - col * lrow
                x[b] = x[b] - col * xrow
    for b in range(nblk):
        x_ref[b * rows:(b + 1) * rows, :] = x[b]


def chol_inv(a):
    n = a.shape[0]
    return pl.pallas_call(
        _chol_inv_kernel,
        out_shape=(jax.ShapeDtypeStruct((n, n), jnp.float32), jax.ShapeDtypeStruct((n, n), jnp.float32)),
        in_specs=[pl.BlockSpec(memory_space=pltpu.VMEM)],
        out_specs=(pl.BlockSpec(memory_space=pltpu.VMEM), pl.BlockSpec(memory_space=pltpu.VMEM)),
    )(a)

BS = 64
NB = 4
REACH = 4
PANEL = 128
HIGHEST = lax.Precision.HIGHEST


def padded_2(block, sides, width):
    for axis, dim in sides:
        count = lax.axis_size(axis)
        forward = [(i, i + 1) for i in range(count - 1)]
        forward.append((count - 1, 0))
        backward = [(target, source) for source, target in forward]
        low = lax.ppermute(
            lax.slice_in_dim(block, block.shape[dim] - width, None, axis=dim), axis, forward
        )
        high = lax.ppermute(lax.slice_in_dim(block, 0, width, axis=dim), axis, backward)
        block = jnp.concatenate([low, block, high], axis=dim)
    return block


def shifted(array, axis, by):
    length = lax.axis_size(axis)
    pairs = [(i, i + by) for i in range(length) if 0 <= i + by < length]
    return lax.ppermute(array, axis, pairs)


GROUP = 4


def ring_pairs(count, stride, by):
    pairs = []
    for i in range(count):
        place = (i // stride) % GROUP
        pairs.append((i, i + ((place + by) % GROUP - place) * stride))
    return pairs


def scatter_sum(data, stride):
    count = lax.axis_size("row")
    place = (lax.axis_index("row") // stride) % GROUP
    chunks = data.reshape(GROUP, data.shape[0] // GROUP, data.shape[1])
    total = lax.dynamic_index_in_dim(chunks, place, 0, keepdims=False)
    for by in range(1, GROUP):
        sent = lax.dynamic_index_in_dim(chunks, (place + by) % GROUP, 0, keepdims=False)
        total = total + lax.ppermute(sent, "row", ring_pairs(count, stride, by))
    return total


def gather_all(piece, stride):
    count = lax.axis_size("row")
    place = (lax.axis_index("row") // stride) % GROUP
    parts = [piece] + [
        lax.ppermute(piece, "row", ring_pairs(count, stride, by)) for by in range(1, GROUP)
    ]
    order = [parts[0]] + parts[:0:-1]
    doubled = jnp.stack(order + order)
    picked = lax.dynamic_slice_in_dim(doubled, (GROUP - place) % GROUP, GROUP, axis=0)
    return picked.reshape(GROUP * piece.shape[0], piece.shape[1])


def row_sum(data):
    inner = scatter_sum(data, 1)
    both = scatter_sum(inner, GROUP)
    inner = gather_all(both, GROUP)
    return gather_all(inner, 1)


def times_t(a, b):
    return lax.dot_general(
        a, b, (((1,), (1,)), ((), ())), precision=HIGHEST, preferred_element_type=jnp.float32
    )


def body(basis, arriving, blocks, pattern, growth):
    row_count = basis.shape[1]
    col_count = basis.shape[2]
    row_blocks = row_count // BS
    total_blocks = row_blocks * lax.axis_size("row")
    padded = padded_2(basis[0], (("row", 0),), REACH * BS)
    tile_stack = padded.reshape(row_blocks + 2 * REACH, BS, col_count)
    local_ids = jnp.arange(row_blocks, dtype=jnp.int32)
    own_blocks = lax.axis_index("row") * row_blocks + local_ids
    offsets = (pattern[0] - own_blocks[:, None] + REACH) % total_blocks
    picked = jnp.take(tile_stack, local_ids[:, None] + offsets, axis=0)
    values = blocks[0].reshape(row_blocks, BS, NB, BS)
    propagated = jnp.einsum("rinj,rnjk->rik", values, picked, preferred_element_type=jnp.float32)
    propagated = propagated.reshape(row_count, col_count).astype(jnp.bfloat16)
    wide_rows = propagated.astype(jnp.float32)
    scale = 1.0 / (row_count * lax.axis_size("row"))

    width = PANEL
    panels = col_count // width
    eye = jnp.eye(width, dtype=jnp.float32)
    parts = [
        lax.dot_general(
            propagated[:, k * width:],
            propagated[:, k * width:(k + 1) * width],
            (((0,), (0,)), ((), ())),
            preferred_element_type=jnp.float32,
        )
        for k in range(panels)
    ]
    packed = row_sum(jnp.concatenate(parts, axis=0)) * scale
    columns = []
    solved = []
    logs = []
    start = 0
    for k in range(panels):
        low = k * width
        panel = packed[start:start + col_count - low]
        start += col_count - low
        if k:
            left = jnp.concatenate(
                [column[low - j * width:] for j, column in enumerate(columns)], axis=1
            )
            panel = panel - times_t(left, left[:width])
        block = panel[:width]
        upper, inverse = chol_inv((block + block.T) * 0.5)
        diag = upper.T
        logs.append(jnp.log(jnp.sum(diag * eye, axis=0)))
        if low + width < col_count:
            below = times_t(panel[width:], inverse)
            columns.append(jnp.concatenate([diag, below], axis=0))
        else:
            columns.append(diag)
        rhs = wide_rows[:, low:low + width]
        if k:
            rhs = rhs - times_t(jnp.concatenate(solved, axis=1), left[:width])
        solved.append(times_t(rhs, inverse))

    next_growth = growth + jnp.concatenate(logs)[None, :]
    renewed = jnp.concatenate(solved, axis=1)
    first_section = lax.axis_index("seg") == 0
    received = shifted(renewed.astype(jnp.bfloat16)[None], "seg", 1)
    next_basis = jnp.where(first_section, arriving[None], received)
    return (next_basis, next_growth)


def solution(mesh):
    return jax.shard_map(
        body,
        mesh=mesh,
        in_specs=(
            P("seg", "row", None),
            P("row", None),
            P("seg", "row", None),
            P("seg", "row", None),
            P("seg", None),
        ),
        out_specs=(P("seg", "row", None), P("seg", None)),
        check_vma=False,
    )
```

```python
import jax
import jax.numpy as jnp
from jax import lax
from jax.sharding import PartitionSpec as P
from jax.experimental import pallas as pl
from jax.experimental.pallas import tpu as pltpu


def _chol_inv_kernel(a_ref, lt_ref, x_ref):
    n = a_ref.shape[0]
    rows = 8
    nblk = n // rows
    a = [a_ref[b * rows:(b + 1) * rows, :] for b in range(nblk)]
    sub = lax.broadcasted_iota(jnp.int32, (rows, n), 0)
    lane1 = lax.broadcasted_iota(jnp.int32, (1, n), 1)
    x = [jnp.where(sub + b * rows == lax.broadcasted_iota(jnp.int32, (rows, n), 1), 1.0, 0.0).astype(jnp.float32)
         for b in range(nblk)]
    for j in range(n):
        bj, r = divmod(j, rows)
        row = a[bj][r:r + 1, :]
        d = row[:, j:j + 1]
        s = lax.rsqrt(d)
        lrow = jnp.where(lane1 >= j, row * s, 0.0)
        lt_ref[j:j + 1, :] = lrow
        xrow = x[bj][r:r + 1, :] * s
        for b in range(bj, nblk):
            col = a[b][:, j:j + 1] * s
            if b == bj:
                keep = sub >= r
                a[b] = jnp.where(keep, a[b] - col * lrow, a[b])
                x[b] = jnp.where(sub == r, xrow, jnp.where(sub > r, x[b] - col * xrow, x[b]))
            else:
                a[b] = a[b] - col * lrow
                x[b] = x[b] - col * xrow
    for b in range(nblk):
        x_ref[b * rows:(b + 1) * rows, :] = x[b]


def chol_inv(a):
    n = a.shape[0]
    return pl.pallas_call(
        _chol_inv_kernel,
        out_shape=(jax.ShapeDtypeStruct((n, n), jnp.float32), jax.ShapeDtypeStruct((n, n), jnp.float32)),
        in_specs=[pl.BlockSpec(memory_space=pltpu.VMEM)],
        out_specs=(pl.BlockSpec(memory_space=pltpu.VMEM), pl.BlockSpec(memory_space=pltpu.VMEM)),
    )(a)

BS = 64
NB = 4
REACH = 4
PANEL = 128
HIGHEST = lax.Precision.HIGHEST


def padded_2(block, sides, width):
    for axis, dim in sides:
        count = lax.axis_size(axis)
        forward = [(i, i + 1) for i in range(count - 1)]
        forward.append((count - 1, 0))
        backward = [(target, source) for source, target in forward]
        low = lax.ppermute(
            lax.slice_in_dim(block, block.shape[dim] - width, None, axis=dim), axis, forward
        )
        high = lax.ppermute(lax.slice_in_dim(block, 0, width, axis=dim), axis, backward)
        block = jnp.concatenate([low, block, high], axis=dim)
    return block


def shifted(array, axis, by):
    length = lax.axis_size(axis)
    pairs = [(i, i + by) for i in range(length) if 0 <= i + by < length]
    return lax.ppermute(array, axis, pairs)


GROUP = 4


def ring_pairs(count, stride, by):
    pairs = []
    for i in range(count):
        place = (i // stride) % GROUP
        pairs.append((i, i + ((place + by) % GROUP - place) * stride))
    return pairs


def scatter_sum(data, stride):
    count = lax.axis_size("row")
    place = (lax.axis_index("row") // stride) % GROUP
    chunks = data.reshape(GROUP, data.shape[0] // GROUP, data.shape[1])
    total = lax.dynamic_index_in_dim(chunks, place, 0, keepdims=False)
    for by in range(1, GROUP):
        sent = lax.dynamic_index_in_dim(chunks, (place + by) % GROUP, 0, keepdims=False)
        total = total + lax.ppermute(sent, "row", ring_pairs(count, stride, by))
    return total


def gather_all(piece, stride):
    count = lax.axis_size("row")
    place = (lax.axis_index("row") // stride) % GROUP
    parts = [piece] + [
        lax.ppermute(piece, "row", ring_pairs(count, stride, by)) for by in range(1, GROUP)
    ]
    order = [parts[0]] + parts[:0:-1]
    doubled = jnp.stack(order + order)
    picked = lax.dynamic_slice_in_dim(doubled, (GROUP - place) % GROUP, GROUP, axis=0)
    return picked.reshape(GROUP * piece.shape[0], piece.shape[1])


def row_sum(data):
    count = lax.axis_size("row")
    chunks = data.reshape(count, data.shape[0] // count, data.shape[1])
    received = lax.all_to_all(chunks, "row", 0, 0)
    total = received[0]
    for j in range(1, count):
        total = total + received[j]
    spread = jnp.broadcast_to(total[None], chunks.shape)
    return lax.all_to_all(spread, "row", 0, 0).reshape(data.shape)


def times_t(a, b):
    return lax.dot_general(
        a, b, (((1,), (1,)), ((), ())), precision=HIGHEST, preferred_element_type=jnp.float32
    )


def body(basis, arriving, blocks, pattern, growth):
    row_count = basis.shape[1]
    col_count = basis.shape[2]
    row_blocks = row_count // BS
    total_blocks = row_blocks * lax.axis_size("row")
    padded = padded_2(basis[0], (("row", 0),), REACH * BS)
    tile_stack = padded.reshape(row_blocks + 2 * REACH, BS, col_count)
    local_ids = jnp.arange(row_blocks, dtype=jnp.int32)
    own_blocks = lax.axis_index("row") * row_blocks + local_ids
    offsets = (pattern[0] - own_blocks[:, None] + REACH) % total_blocks
    picked = jnp.take(tile_stack, local_ids[:, None] + offsets, axis=0)
    values = blocks[0].reshape(row_blocks, BS, NB, BS)
    propagated = jnp.einsum("rinj,rnjk->rik", values, picked, preferred_element_type=jnp.float32)
    propagated = propagated.reshape(row_count, col_count).astype(jnp.bfloat16)
    wide_rows = propagated.astype(jnp.float32)
    scale = 1.0 / (row_count * lax.axis_size("row"))

    width = PANEL
    panels = col_count // width
    eye = jnp.eye(width, dtype=jnp.float32)
    parts = [
        lax.dot_general(
            propagated[:, k * width:],
            propagated[:, k * width:(k + 1) * width],
            (((0,), (0,)), ((), ())),
            preferred_element_type=jnp.float32,
        )
        for k in range(panels)
    ]
    packed = row_sum(jnp.concatenate(parts, axis=0)) * scale
    columns = []
    solved = []
    logs = []
    start = 0
    for k in range(panels):
        low = k * width
        panel = packed[start:start + col_count - low]
        start += col_count - low
        if k:
            left = jnp.concatenate(
                [column[low - j * width:] for j, column in enumerate(columns)], axis=1
            )
            panel = panel - times_t(left, left[:width])
        block = panel[:width]
        upper, inverse = chol_inv((block + block.T) * 0.5)
        diag = upper.T
        logs.append(jnp.log(jnp.sum(diag * eye, axis=0)))
        if low + width < col_count:
            below = times_t(panel[width:], inverse)
            columns.append(jnp.concatenate([diag, below], axis=0))
        else:
            columns.append(diag)
        rhs = wide_rows[:, low:low + width]
        if k:
            rhs = rhs - times_t(jnp.concatenate(solved, axis=1), left[:width])
        solved.append(times_t(rhs, inverse))

    next_growth = growth + jnp.concatenate(logs)[None, :]
    renewed = jnp.concatenate(solved, axis=1)
    first_section = lax.axis_index("seg") == 0
    received = shifted(renewed.astype(jnp.bfloat16)[None], "seg", 1)
    next_basis = jnp.where(first_section, arriving[None], received)
    return (next_basis, next_growth)


def solution(mesh):
    return jax.shard_map(
        body,
        mesh=mesh,
        in_specs=(
            P("seg", "row", None),
            P("row", None),
            P("seg", "row", None),
            P("seg", "row", None),
            P("seg", None),
        ),
        out_specs=(P("seg", "row", None), P("seg", None)),
        check_vma=False,
    )
```

```python
import jax
import jax.numpy as jnp
from jax import lax
from jax.sharding import PartitionSpec as P
from jax.experimental import pallas as pl
from jax.experimental.pallas import tpu as pltpu


def _chol_inv_kernel(a_ref, l_ref, x_ref, lt_ref):
    n = a_ref.shape[0]
    rows = 8
    nblk = n // rows
    whole = a_ref[...]
    whole = (whole + whole.T) * 0.5
    a = [whole[b * rows:(b + 1) * rows, :] for b in range(nblk)]
    sub = lax.broadcasted_iota(jnp.int32, (rows, n), 0)
    lane1 = lax.broadcasted_iota(jnp.int32, (1, n), 1)
    x = [jnp.where(sub + b * rows == lax.broadcasted_iota(jnp.int32, (rows, n), 1), 1.0, 0.0).astype(jnp.float32)
         for b in range(nblk)]
    for j in range(n):
        bj, r = divmod(j, rows)
        row = a[bj][r:r + 1, :]
        d = row[:, j:j + 1]
        s = lax.rsqrt(d)
        lrow = jnp.where(lane1 >= j, row * s, 0.0)
        lt_ref[j:j + 1, :] = lrow
        xrow = x[bj][r:r + 1, :] * s
        for b in range(bj, nblk):
            col = a[b][:, j:j + 1] * s
            if b == bj:
                keep = sub >= r
                a[b] = jnp.where(keep, a[b] - col * lrow, a[b])
                x[b] = jnp.where(sub == r, xrow, jnp.where(sub > r, x[b] - col * xrow, x[b]))
            else:
                a[b] = a[b] - col * lrow
                x[b] = x[b] - col * xrow
    for b in range(nblk):
        x_ref[b * rows:(b + 1) * rows, :] = x[b]
    l_ref[...] = lt_ref[...].T


def chol_inv(a):
    n = a.shape[0]
    return pl.pallas_call(
        _chol_inv_kernel,
        out_shape=(jax.ShapeDtypeStruct((n, n), jnp.float32), jax.ShapeDtypeStruct((n, n), jnp.float32)),
        in_specs=[pl.BlockSpec(memory_space=pltpu.VMEM)],
        out_specs=(pl.BlockSpec(memory_space=pltpu.VMEM), pl.BlockSpec(memory_space=pltpu.VMEM)),
        scratch_shapes=[pltpu.VMEM((n, n), jnp.float32)],
    )(a)


BS = 64
NB = 4
REACH = 4
PANEL = 128
HIGH = lax.Precision.HIGH


def padded_2(block, sides, width):
    for axis, dim in sides:
        count = lax.axis_size(axis)
        forward = [(i, i + 1) for i in range(count - 1)]
        forward.append((count - 1, 0))
        backward = [(target, source) for source, target in forward]
        low = lax.ppermute(
            lax.slice_in_dim(block, block.shape[dim] - width, None, axis=dim), axis, forward
        )
        high = lax.ppermute(lax.slice_in_dim(block, 0, width, axis=dim), axis, backward)
        block = jnp.concatenate([low, block, high], axis=dim)
    return block


def shifted(array, axis, by):
    length = lax.axis_size(axis)
    pairs = [(i, i + by) for i in range(length) if 0 <= i + by < length]
    return lax.ppermute(array, axis, pairs)


GROUP = 4


def ring_pairs(count, stride, by):
    pairs = []
    for i in range(count):
        place = (i // stride) % GROUP
        pairs.append((i, i + ((place + by) % GROUP - place) * stride))
    return pairs


def scatter_sum(data, stride):
    count = lax.axis_size("row")
    place = (lax.axis_index("row") // stride) % GROUP
    chunks = data.reshape(GROUP, data.shape[0] // GROUP, data.shape[1])
    total = lax.dynamic_index_in_dim(chunks, place, 0, keepdims=False)
    for by in range(1, GROUP):
        sent = lax.dynamic_index_in_dim(chunks, (place + by) % GROUP, 0, keepdims=False)
        total = total + lax.ppermute(sent, "row", ring_pairs(count, stride, by))
    return total


def gather_all(piece, stride):
    count = lax.axis_size("row")
    place = (lax.axis_index("row") // stride) % GROUP
    parts = [piece] + [
        lax.ppermute(piece, "row", ring_pairs(count, stride, by)) for by in range(1, GROUP)
    ]
    order = [parts[0]] + parts[:0:-1]
    doubled = jnp.stack(order + order)
    picked = lax.dynamic_slice_in_dim(doubled, (GROUP - place) % GROUP, GROUP, axis=0)
    return picked.reshape(GROUP * piece.shape[0], piece.shape[1])


def row_sum(data):
    count = lax.axis_size("row")
    chunks = data.reshape(count, data.shape[0] // count, data.shape[1])
    received = lax.all_to_all(chunks, "row", 0, 0)
    total = received[0]
    for j in range(1, count):
        total = total + received[j]
    spread = jnp.broadcast_to(total[None], chunks.shape)
    return lax.all_to_all(spread, "row", 0, 0).reshape(data.shape)


def times_t(a, b):
    return lax.dot_general(
        a, b, (((1,), (1,)), ((), ())), precision=HIGH, preferred_element_type=jnp.float32
    )


def body(basis, arriving, blocks, pattern, growth):
    row_count = basis.shape[1]
    col_count = basis.shape[2]
    row_blocks = row_count // BS
    total_blocks = row_blocks * lax.axis_size("row")
    padded = padded_2(basis[0], (("row", 0),), REACH * BS)
    tile_stack = padded.reshape(row_blocks + 2 * REACH, BS, col_count)
    local_ids = jnp.arange(row_blocks, dtype=jnp.int32)
    own_blocks = lax.axis_index("row") * row_blocks + local_ids
    offsets = (pattern[0] - own_blocks[:, None] + REACH) % total_blocks
    picked = jnp.take(tile_stack, local_ids[:, None] + offsets, axis=0)
    values = blocks[0].reshape(row_blocks, BS, NB, BS)
    propagated = jnp.einsum("rinj,rnjk->rik", values, picked, preferred_element_type=jnp.float32)
    propagated = propagated.reshape(row_count, col_count).astype(jnp.bfloat16)
    wide_rows = propagated.astype(jnp.float32)
    scale = 1.0 / (row_count * lax.axis_size("row"))

    width = PANEL
    panels = col_count // width
    eye = jnp.eye(width, dtype=jnp.float32)
    parts = [
        lax.dot_general(
            propagated[:, k * width:],
            propagated[:, k * width:(k + 1) * width],
            (((0,), (0,)), ((), ())),
            preferred_element_type=jnp.float32,
        )
        for k in range(panels)
    ]
    packed = row_sum(jnp.concatenate(parts, axis=0)) * scale
    columns = []
    solved = []
    logs = []
    start = 0
    for k in range(panels):
        low = k * width
        panel = packed[start:start + col_count - low]
        start += col_count - low
        if k:
            left = jnp.concatenate(
                [column[low - j * width:] for j, column in enumerate(columns)], axis=1
            )
            panel = panel - times_t(left, left[:width])
        diag, inverse = chol_inv(panel[:width])
        logs.append(jnp.log(jnp.sum(diag * eye, axis=0)))
        if low + width < col_count:
            below = times_t(panel[width:], inverse)
            columns.append(jnp.concatenate([diag, below], axis=0))
        else:
            columns.append(diag)
        rhs = wide_rows[:, low:low + width]
        if k:
            rhs = rhs - times_t(jnp.concatenate(solved, axis=1), left[:width])
        solved.append(times_t(rhs, inverse))

    next_growth = growth + jnp.concatenate(logs)[None, :]
    renewed = jnp.concatenate(solved, axis=1)
    first_section = lax.axis_index("seg") == 0
    received = shifted(renewed.astype(jnp.bfloat16)[None], "seg", 1)
    next_basis = jnp.where(first_section, arriving[None], received)
    return (next_basis, next_growth)


def solution(mesh):
    return jax.shard_map(
        body,
        mesh=mesh,
        in_specs=(
            P("seg", "row", None),
            P("row", None),
            P("seg", "row", None),
            P("seg", "row", None),
            P("seg", None),
        ),
        out_specs=(P("seg", "row", None), P("seg", None)),
        check_vma=False,
    )
```

```python
import jax
import jax.numpy as jnp
from jax import lax
from jax.sharding import PartitionSpec as P
from jax.experimental import pallas as pl
from jax.experimental.pallas import tpu as pltpu


def _chol_inv_kernel(a_ref, l_ref, x_ref, lt_ref):
    n = a_ref.shape[0]
    rows = 8
    nblk = n // rows
    whole = a_ref[...]
    whole = (whole + whole.T) * 0.5
    a = [whole[b * rows:(b + 1) * rows, :] for b in range(nblk)]
    sub = lax.broadcasted_iota(jnp.int32, (rows, n), 0)
    lane1 = lax.broadcasted_iota(jnp.int32, (1, n), 1)
    x = [jnp.where(sub + b * rows == lax.broadcasted_iota(jnp.int32, (rows, n), 1), 1.0, 0.0).astype(jnp.float32)
         for b in range(nblk)]
    for j in range(n):
        bj, r = divmod(j, rows)
        row = a[bj][r:r + 1, :]
        d = row[:, j:j + 1]
        s = lax.rsqrt(d)
        lrow = jnp.where(lane1 >= j, row * s, 0.0)
        lt_ref[j:j + 1, :] = lrow
        xrow = x[bj][r:r + 1, :] * s
        for b in range(bj, nblk):
            col = a[b][:, j:j + 1] * s
            if b == bj:
                keep = sub >= r
                a[b] = jnp.where(keep, a[b] - col * lrow, a[b])
                x[b] = jnp.where(sub == r, xrow, jnp.where(sub > r, x[b] - col * xrow, x[b]))
            else:
                a[b] = a[b] - col * lrow
                x[b] = x[b] - col * xrow
    for b in range(nblk):
        x_ref[b * rows:(b + 1) * rows, :] = x[b]
    l_ref[...] = lt_ref[...].T


def chol_inv(a):
    n = a.shape[0]
    return pl.pallas_call(
        _chol_inv_kernel,
        out_shape=(jax.ShapeDtypeStruct((n, n), jnp.float32), jax.ShapeDtypeStruct((n, n), jnp.float32)),
        in_specs=[pl.BlockSpec(memory_space=pltpu.VMEM)],
        out_specs=(pl.BlockSpec(memory_space=pltpu.VMEM), pl.BlockSpec(memory_space=pltpu.VMEM)),
        scratch_shapes=[pltpu.VMEM((n, n), jnp.float32)],
    )(a)


BS = 64
NB = 4
REACH = 4
PANEL = 128
HIGH = lax.Precision.HIGH


def padded_2(block, sides, width):
    for axis, dim in sides:
        count = lax.axis_size(axis)
        forward = [(i, i + 1) for i in range(count - 1)]
        forward.append((count - 1, 0))
        backward = [(target, source) for source, target in forward]
        low = lax.ppermute(
            lax.slice_in_dim(block, block.shape[dim] - width, None, axis=dim), axis, forward
        )
        high = lax.ppermute(lax.slice_in_dim(block, 0, width, axis=dim), axis, backward)
        block = jnp.concatenate([low, block, high], axis=dim)
    return block


def shifted(array, axis, by):
    length = lax.axis_size(axis)
    pairs = [(i, i + by) for i in range(length) if 0 <= i + by < length]
    return lax.ppermute(array, axis, pairs)


GROUP = 4


def ring_pairs(count, stride, by):
    pairs = []
    for i in range(count):
        place = (i // stride) % GROUP
        pairs.append((i, i + ((place + by) % GROUP - place) * stride))
    return pairs


def scatter_sum(data, stride):
    count = lax.axis_size("row")
    place = (lax.axis_index("row") // stride) % GROUP
    chunks = data.reshape(GROUP, data.shape[0] // GROUP, data.shape[1])
    total = lax.dynamic_index_in_dim(chunks, place, 0, keepdims=False)
    for by in range(1, GROUP):
        sent = lax.dynamic_index_in_dim(chunks, (place + by) % GROUP, 0, keepdims=False)
        total = total + lax.ppermute(sent, "row", ring_pairs(count, stride, by))
    return total


def gather_all(piece, stride):
    count = lax.axis_size("row")
    place = (lax.axis_index("row") // stride) % GROUP
    parts = [piece] + [
        lax.ppermute(piece, "row", ring_pairs(count, stride, by)) for by in range(1, GROUP)
    ]
    order = [parts[0]] + parts[:0:-1]
    doubled = jnp.stack(order + order)
    picked = lax.dynamic_slice_in_dim(doubled, (GROUP - place) % GROUP, GROUP, axis=0)
    return picked.reshape(GROUP * piece.shape[0], piece.shape[1])


def row_sum(data):
    count = lax.axis_size("row")
    chunks = data.reshape(count, data.shape[0] // count, data.shape[1])
    received = lax.all_to_all(chunks, "row", 0, 0)
    total = received[0]
    for j in range(1, count):
        total = total + received[j]
    spread = jnp.broadcast_to(total[None], chunks.shape)
    return lax.all_to_all(spread, "row", 0, 0).reshape(data.shape)


def times_t(a, b):
    return lax.dot_general(
        a, b, (((1,), (1,)), ((), ())), precision=HIGH, preferred_element_type=jnp.float32
    )


def body(basis, arriving, blocks, pattern, growth):
    row_count = basis.shape[1]
    col_count = basis.shape[2]
    row_blocks = row_count // BS
    total_blocks = row_blocks * lax.axis_size("row")
    padded = padded_2(basis[0], (("row", 0),), REACH * BS)
    tile_stack = padded.reshape(row_blocks + 2 * REACH, BS, col_count)
    local_ids = jnp.arange(row_blocks, dtype=jnp.int32)
    own_blocks = lax.axis_index("row") * row_blocks + local_ids
    offsets = (pattern[0] - own_blocks[:, None] + REACH) % total_blocks
    picked = jnp.take(tile_stack, local_ids[:, None] + offsets, axis=0)
    values = blocks[0].reshape(row_blocks, BS, NB, BS)
    propagated = jnp.einsum("rinj,rnjk->rik", values, picked, preferred_element_type=jnp.float32)
    propagated = propagated.reshape(row_count, col_count).astype(jnp.bfloat16)
    wide_rows = propagated.astype(jnp.float32)
    scale = 1.0 / (row_count * lax.axis_size("row"))

    width = PANEL
    panels = col_count // width
    eye = jnp.eye(width, dtype=jnp.float32)
    parts = [
        lax.dot_general(
            propagated[:, k * width:],
            propagated[:, k * width:(k + 1) * width],
            (((0,), (0,)), ((), ())),
            preferred_element_type=jnp.float32,
        )
        for k in range(panels)
    ]
    packed = row_sum(jnp.concatenate(parts, axis=0)) * scale
    factor = jnp.zeros((col_count, col_count), jnp.float32)
    solved = jnp.zeros(wide_rows.shape, jnp.float32)
    logs = []
    start = 0
    for k in range(panels):
        low = k * width
        high = low + width
        panel = packed[start:start + col_count - low]
        start += col_count - low
        if k:
            panel = panel - times_t(factor[low:, :low], factor[low:high, :low])
        diag, inverse = chol_inv(panel[:width])
        logs.append(jnp.log(jnp.sum(diag * eye, axis=0)))
        if high < col_count:
            below = times_t(panel[width:], inverse)
            factor = lax.dynamic_update_slice(
                factor, jnp.concatenate([diag, below], axis=0), (low, low)
            )
        else:
            factor = lax.dynamic_update_slice(factor, diag, (low, low))
        rhs = wide_rows[:, low:high]
        if k:
            rhs = rhs - times_t(solved[:, :low], factor[low:high, :low])
        solved = lax.dynamic_update_slice(solved, times_t(rhs, inverse), (0, low))

    next_growth = growth + jnp.concatenate(logs)[None, :]
    renewed = solved
    first_section = lax.axis_index("seg") == 0
    received = shifted(renewed.astype(jnp.bfloat16)[None], "seg", 1)
    next_basis = jnp.where(first_section, arriving[None], received)
    return (next_basis, next_growth)


def solution(mesh):
    return jax.shard_map(
        body,
        mesh=mesh,
        in_specs=(
            P("seg", "row", None),
            P("row", None),
            P("seg", "row", None),
            P("seg", "row", None),
            P("seg", None),
        ),
        out_specs=(P("seg", "row", None), P("seg", None)),
        check_vma=False,
    )
```

```python
import jax
import jax.numpy as jnp
from jax import lax
from jax.sharding import PartitionSpec as P
from jax.experimental import pallas as pl
from jax.experimental.pallas import tpu as pltpu


def _chol_inv_kernel(a_ref, l_ref, x_ref, g_ref, lt_ref):
    n = a_ref.shape[0]
    rows = 8
    nblk = n // rows
    whole = a_ref[...]
    whole = (whole + whole.T) * 0.5
    a = [whole[b * rows:(b + 1) * rows, :] for b in range(nblk)]
    sub = lax.broadcasted_iota(jnp.int32, (rows, n), 0)
    lane1 = lax.broadcasted_iota(jnp.int32, (1, n), 1)
    x = [jnp.where(sub + b * rows == lax.broadcasted_iota(jnp.int32, (rows, n), 1), 1.0, 0.0).astype(jnp.float32)
         for b in range(nblk)]
    diag = jnp.ones((1, n), jnp.float32)
    for j in range(n):
        bj, r = divmod(j, rows)
        row = a[bj][r:r + 1, :]
        d = row[:, j:j + 1]
        s = lax.rsqrt(d)
        lrow = jnp.where(lane1 >= j, row * s, 0.0)
        diag = jnp.where(lane1 == j, lrow, diag)
        lt_ref[j:j + 1, :] = lrow
        xrow = x[bj][r:r + 1, :] * s
        for b in range(bj, nblk):
            col = a[b][:, j:j + 1] * s
            if b == bj:
                keep = sub >= r
                a[b] = jnp.where(keep, a[b] - col * lrow, a[b])
                x[b] = jnp.where(sub == r, xrow, jnp.where(sub > r, x[b] - col * xrow, x[b]))
            else:
                a[b] = a[b] - col * lrow
                x[b] = x[b] - col * xrow
    for b in range(nblk):
        x_ref[b * rows:(b + 1) * rows, :] = x[b]
    l_ref[...] = lt_ref[...].T
    g_ref[...] = jnp.log(diag)


def chol_inv(a):
    n = a.shape[0]
    return pl.pallas_call(
        _chol_inv_kernel,
        out_shape=(
            jax.ShapeDtypeStruct((n, n), jnp.float32),
            jax.ShapeDtypeStruct((n, n), jnp.float32),
            jax.ShapeDtypeStruct((1, n), jnp.float32),
        ),
        in_specs=[pl.BlockSpec(memory_space=pltpu.VMEM)],
        out_specs=(
            pl.BlockSpec(memory_space=pltpu.VMEM),
            pl.BlockSpec(memory_space=pltpu.VMEM),
            pl.BlockSpec(memory_space=pltpu.VMEM),
        ),
        scratch_shapes=[pltpu.VMEM((n, n), jnp.float32)],
    )(a)


BS = 64
NB = 4
REACH = 4
PANEL = 128
HIGH = lax.Precision.HIGH


def padded_2(block, sides, width):
    for axis, dim in sides:
        count = lax.axis_size(axis)
        forward = [(i, i + 1) for i in range(count - 1)]
        forward.append((count - 1, 0))
        backward = [(target, source) for source, target in forward]
        low = lax.ppermute(
            lax.slice_in_dim(block, block.shape[dim] - width, None, axis=dim), axis, forward
        )
        high = lax.ppermute(lax.slice_in_dim(block, 0, width, axis=dim), axis, backward)
        block = jnp.concatenate([low, block, high], axis=dim)
    return block


def shifted(array, axis, by):
    length = lax.axis_size(axis)
    pairs = [(i, i + by) for i in range(length) if 0 <= i + by < length]
    return lax.ppermute(array, axis, pairs)


GROUP = 4


def ring_pairs(count, stride, by):
    pairs = []
    for i in range(count):
        place = (i // stride) % GROUP
        pairs.append((i, i + ((place + by) % GROUP - place) * stride))
    return pairs


def scatter_sum(data, stride):
    count = lax.axis_size("row")
    place = (lax.axis_index("row") // stride) % GROUP
    chunks = data.reshape(GROUP, data.shape[0] // GROUP, data.shape[1])
    total = lax.dynamic_index_in_dim(chunks, place, 0, keepdims=False)
    for by in range(1, GROUP):
        sent = lax.dynamic_index_in_dim(chunks, (place + by) % GROUP, 0, keepdims=False)
        total = total + lax.ppermute(sent, "row", ring_pairs(count, stride, by))
    return total


def gather_all(piece, stride):
    count = lax.axis_size("row")
    place = (lax.axis_index("row") // stride) % GROUP
    parts = [piece] + [
        lax.ppermute(piece, "row", ring_pairs(count, stride, by)) for by in range(1, GROUP)
    ]
    order = [parts[0]] + parts[:0:-1]
    doubled = jnp.stack(order + order)
    picked = lax.dynamic_slice_in_dim(doubled, (GROUP - place) % GROUP, GROUP, axis=0)
    return picked.reshape(GROUP * piece.shape[0], piece.shape[1])


def row_sum(data):
    count = lax.axis_size("row")
    chunks = data.reshape(count, data.shape[0] // count, data.shape[1])
    received = lax.all_to_all(chunks, "row", 0, 0)
    total = received[0]
    for j in range(1, count):
        total = total + received[j]
    spread = jnp.broadcast_to(total[None], chunks.shape)
    return lax.all_to_all(spread, "row", 0, 0).reshape(data.shape)


def times_t(a, b):
    return lax.dot_general(
        a, b, (((1,), (1,)), ((), ())), precision=HIGH, preferred_element_type=jnp.float32
    )


def body(basis, arriving, blocks, pattern, growth):
    row_count = basis.shape[1]
    col_count = basis.shape[2]
    row_blocks = row_count // BS
    total_blocks = row_blocks * lax.axis_size("row")
    padded = padded_2(basis[0], (("row", 0),), REACH * BS)
    tile_stack = padded.reshape(row_blocks + 2 * REACH, BS, col_count)
    local_ids = jnp.arange(row_blocks, dtype=jnp.int32)
    own_blocks = lax.axis_index("row") * row_blocks + local_ids
    offsets = (pattern[0] - own_blocks[:, None] + REACH) % total_blocks
    picked = jnp.take(tile_stack, local_ids[:, None] + offsets, axis=0)
    values = blocks[0].reshape(row_blocks, BS, NB, BS)
    propagated = jnp.einsum("rinj,rnjk->rik", values, picked, preferred_element_type=jnp.float32)
    propagated = propagated.reshape(row_count, col_count).astype(jnp.bfloat16)
    wide_rows = propagated.astype(jnp.float32)
    scale = 1.0 / (row_count * lax.axis_size("row"))

    width = PANEL
    panels = col_count // width
    parts = [
        lax.dot_general(
            propagated[:, k * width:],
            propagated[:, k * width:(k + 1) * width],
            (((0,), (0,)), ((), ())),
            preferred_element_type=jnp.float32,
        )
        for k in range(panels)
    ]
    packed = row_sum(jnp.concatenate(parts, axis=0)) * scale
    factor = jnp.zeros((col_count, col_count), jnp.float32)
    solved = jnp.zeros(wide_rows.shape, jnp.float32)
    logs = []
    start = 0
    for k in range(panels):
        low = k * width
        high = low + width
        panel = packed[start:start + col_count - low]
        start += col_count - low
        if k:
            panel = panel - times_t(factor[low:, :low], factor[low:high, :low])
        diag, inverse, log_diag = chol_inv(panel[:width])
        logs.append(log_diag)
        if high < col_count:
            below = times_t(panel[width:], inverse)
            factor = lax.dynamic_update_slice(
                factor, jnp.concatenate([diag, below], axis=0), (low, low)
            )
        else:
            factor = lax.dynamic_update_slice(factor, diag, (low, low))
        rhs = wide_rows[:, low:high]
        if k:
            rhs = rhs - times_t(solved[:, :low], factor[low:high, :low])
        solved = lax.dynamic_update_slice(solved, times_t(rhs, inverse), (0, low))

    next_growth = growth + jnp.concatenate(logs, axis=1)
    renewed = solved
    first_section = lax.axis_index("seg") == 0
    received = shifted(renewed.astype(jnp.bfloat16)[None], "seg", 1)
    next_basis = jnp.where(first_section, arriving[None], received)
    return (next_basis, next_growth)


def solution(mesh):
    return jax.shard_map(
        body,
        mesh=mesh,
        in_specs=(
            P("seg", "row", None),
            P("row", None),
            P("seg", "row", None),
            P("seg", "row", None),
            P("seg", None),
        ),
        out_specs=(P("seg", "row", None), P("seg", None)),
        check_vma=False,
    )
```

```python
import jax
import jax.numpy as jnp
from jax import lax
from jax.sharding import PartitionSpec as P
from jax.experimental import pallas as pl
from jax.experimental.pallas import tpu as pltpu


def _chol_inv_kernel(a_ref, l_ref, x_ref, g_ref, lt_ref):
    n = a_ref.shape[1]
    rows = 8
    nblk = n // rows
    whole = a_ref[...]
    whole = (whole + whole.T) * 0.5
    a = [whole[b * rows:(b + 1) * rows, :] for b in range(nblk)]
    sub = lax.broadcasted_iota(jnp.int32, (rows, n), 0)
    lane1 = lax.broadcasted_iota(jnp.int32, (1, n), 1)
    x = [jnp.where(sub + b * rows == lax.broadcasted_iota(jnp.int32, (rows, n), 1), 1.0, 0.0).astype(jnp.float32)
         for b in range(nblk)]
    diag = jnp.ones((1, n), jnp.float32)
    for j in range(n):
        bj, r = divmod(j, rows)
        row = a[bj][r:r + 1, :]
        d = row[:, j:j + 1]
        s = lax.rsqrt(d)
        lrow = jnp.where(lane1 >= j, row * s, 0.0)
        diag = jnp.where(lane1 == j, lrow, diag)
        lt_ref[j:j + 1, :] = lrow
        xrow = x[bj][r:r + 1, :] * s
        for b in range(bj, nblk):
            col = a[b][:, j:j + 1] * s
            a[b] = a[b] - col * lrow
            if b == bj:
                x[b] = jnp.where(sub == r, xrow, jnp.where(sub > r, x[b] - col * xrow, x[b]))
            else:
                x[b] = x[b] - col * xrow
    for b in range(nblk):
        x_ref[b * rows:(b + 1) * rows, :] = x[b]
    l_ref[...] = lt_ref[...].T
    g_ref[...] = jnp.log(diag)


def chol_inv(a):
    n = a.shape[1]
    return pl.pallas_call(
        _chol_inv_kernel,
        out_shape=(
            jax.ShapeDtypeStruct((n, n), jnp.float32),
            jax.ShapeDtypeStruct((n, n), jnp.float32),
            jax.ShapeDtypeStruct((1, n), jnp.float32),
        ),
        grid=(1,),
        in_specs=[pl.BlockSpec((n, n), lambda i: (0, 0))],
        out_specs=(
            pl.BlockSpec(memory_space=pltpu.VMEM),
            pl.BlockSpec(memory_space=pltpu.VMEM),
            pl.BlockSpec(memory_space=pltpu.VMEM),
        ),
        scratch_shapes=[pltpu.VMEM((n, n), jnp.float32)],
    )(a)


BS = 64
NB = 4
REACH = 4
PANEL = 128
HIGH = lax.Precision.HIGH


def padded_2(block, sides, width):
    for axis, dim in sides:
        count = lax.axis_size(axis)
        forward = [(i, i + 1) for i in range(count - 1)]
        forward.append((count - 1, 0))
        backward = [(target, source) for source, target in forward]
        low = lax.ppermute(
            lax.slice_in_dim(block, block.shape[dim] - width, None, axis=dim), axis, forward
        )
        high = lax.ppermute(lax.slice_in_dim(block, 0, width, axis=dim), axis, backward)
        block = jnp.concatenate([low, block, high], axis=dim)
    return block


def shifted(array, axis, by):
    length = lax.axis_size(axis)
    pairs = [(i, i + by) for i in range(length) if 0 <= i + by < length]
    return lax.ppermute(array, axis, pairs)


GROUP = 4


def ring_pairs(count, stride, by):
    pairs = []
    for i in range(count):
        place = (i // stride) % GROUP
        pairs.append((i, i + ((place + by) % GROUP - place) * stride))
    return pairs


def scatter_sum(data, stride):
    count = lax.axis_size("row")
    place = (lax.axis_index("row") // stride) % GROUP
    chunks = data.reshape(GROUP, data.shape[0] // GROUP, data.shape[1])
    total = lax.dynamic_index_in_dim(chunks, place, 0, keepdims=False)
    for by in range(1, GROUP):
        sent = lax.dynamic_index_in_dim(chunks, (place + by) % GROUP, 0, keepdims=False)
        total = total + lax.ppermute(sent, "row", ring_pairs(count, stride, by))
    return total


def gather_all(piece, stride):
    count = lax.axis_size("row")
    place = (lax.axis_index("row") // stride) % GROUP
    parts = [piece] + [
        lax.ppermute(piece, "row", ring_pairs(count, stride, by)) for by in range(1, GROUP)
    ]
    order = [parts[0]] + parts[:0:-1]
    doubled = jnp.stack(order + order)
    picked = lax.dynamic_slice_in_dim(doubled, (GROUP - place) % GROUP, GROUP, axis=0)
    return picked.reshape(GROUP * piece.shape[0], piece.shape[1])


def row_sum(data):
    count = lax.axis_size("row")
    chunks = data.reshape(count, data.shape[0] // count, data.shape[1])
    received = lax.all_to_all(chunks, "row", 0, 0)
    total = received[0]
    for j in range(1, count):
        total = total + received[j]
    spread = jnp.broadcast_to(total[None], chunks.shape)
    return lax.all_to_all(spread, "row", 0, 0).reshape(data.shape)


def times_t(a, b):
    return lax.dot_general(
        a, b, (((1,), (1,)), ((), ())), precision=HIGH, preferred_element_type=jnp.float32
    )


def body(basis, arriving, blocks, pattern, growth):
    row_count = basis.shape[1]
    col_count = basis.shape[2]
    row_blocks = row_count // BS
    total_blocks = row_blocks * lax.axis_size("row")
    padded = padded_2(basis[0], (("row", 0),), REACH * BS)
    tile_stack = padded.reshape(row_blocks + 2 * REACH, BS, col_count)
    local_ids = jnp.arange(row_blocks, dtype=jnp.int32)
    own_blocks = lax.axis_index("row") * row_blocks + local_ids
    offsets = (pattern[0] - own_blocks[:, None] + REACH) % total_blocks
    picked = jnp.take(tile_stack, local_ids[:, None] + offsets, axis=0)
    values = blocks[0].reshape(row_blocks, BS, NB, BS)
    propagated = jnp.einsum("rinj,rnjk->rik", values, picked, preferred_element_type=jnp.float32)
    propagated = propagated.reshape(row_count, col_count).astype(jnp.bfloat16)
    wide_rows = propagated.astype(jnp.float32)
    scale = 1.0 / (row_count * lax.axis_size("row"))

    width = PANEL
    panels = col_count // width
    parts = [
        lax.dot_general(
            propagated[:, k * width:],
            propagated[:, k * width:(k + 1) * width],
            (((0,), (0,)), ((), ())),
            preferred_element_type=jnp.float32,
        )
        for k in range(panels)
    ]
    packed = row_sum(jnp.concatenate(parts, axis=0)) * scale
    factor = jnp.zeros((col_count, col_count), jnp.float32)
    solved = jnp.zeros(wide_rows.shape, jnp.float32)
    logs = []
    start = 0
    for k in range(panels):
        low = k * width
        high = low + width
        panel = packed[start:start + col_count - low]
        start += col_count - low
        if k:
            panel = panel - times_t(factor[low:, :low], factor[low:high, :low])
        diag, inverse, log_diag = chol_inv(panel)
        logs.append(log_diag)
        if high < col_count:
            below = times_t(panel[width:], inverse)
            factor = lax.dynamic_update_slice(factor, below, (high, low))
        factor = lax.dynamic_update_slice(factor, diag, (low, low))
        rhs = wide_rows[:, low:high]
        if k:
            rhs = rhs - times_t(solved[:, :low], factor[low:high, :low])
        solved = lax.dynamic_update_slice(solved, times_t(rhs, inverse), (0, low))

    next_growth = growth + jnp.concatenate(logs, axis=1)
    renewed = solved
    first_section = lax.axis_index("seg") == 0
    received = shifted(renewed.astype(jnp.bfloat16)[None], "seg", 1)
    next_basis = jnp.where(first_section, arriving[None], received)
    return (next_basis, next_growth)


def solution(mesh):
    return jax.shard_map(
        body,
        mesh=mesh,
        in_specs=(
            P("seg", "row", None),
            P("row", None),
            P("seg", "row", None),
            P("seg", "row", None),
            P("seg", None),
        ),
        out_specs=(P("seg", "row", None), P("seg", None)),
        check_vma=False,
    )
```
